32 devices in a mesh: seq: 8 (over y, x, core), chan: 4 (over z).
Axes of the slice: x: 2, y: 2, z: 4, core: 2. Of those that a mesh axis runs over, the one named last changes fastest.
Arguments:
- signal: bfloat16 [512, 8192], P(None, ('seq', 'chan')), may hold values from -6 to 6
- inner_gate: bfloat16 [512, 8192], P(None, ('seq', 'chan')), may hold values from -6 to 6
- outer_gate: bfloat16 [512, 8192], P(None, ('seq', 'chan')), may hold values from -6 to 6
- decay_rate: float32 [512, 16], replicated, may hold values from 3.0517578e-05 to 0.04
- residue: float32 [512, 16], replicated, may hold values from -0.1 to 0.1
- skip_gain: float32 [512], replicated, may hold values from -0.15 to 0.15
Outputs:
- layer_out: bfloat16 [512, 8192], P(None, ('seq', 'chan'))
- modal_state: float32 [512, 16], replicated
The draws below stay inside these ranges and needn't reach their ends.
All inputs are finite; a program needn't handle non-finite values.
Results may differ from the reference program's by a relative error of at most 0.006.
Values may be sent and summed in bfloat16 or wider, within the bound.
No kernel may reach another device: no remote copies, remote signals or barrier semaphores. Data moves between devices by JAX's collectives and lax.ppermute only.
A program may use at most 64 MiB of HBM per device.

```python
import math
import jax
import jax.numpy as jnp
from jax import lax

CHANNELS = 512
MODES = 16
LENGTH = 8192


def channel_kind(key):
    return jax.random.randint(jax.random.fold_in(key, 11), (CHANNELS,), 0, 3)


def mode_table(key):
    kinds = channel_kind(key)[:, None]
    choose = jax.random.uniform(jax.random.fold_in(key, 12), (CHANNELS, MODES), jnp.float32)
    lasting = choose < 0.25
    spread_u = jax.random.uniform(jax.random.fold_in(key, 13), (CHANNELS, MODES), jnp.float32)
    rate_fast = 0.02 + 0.02 * spread_u
    rate_slow = 0.0015 * jnp.exp(math.log(2.0) * spread_u)
    rate_tone = 0.02 + 0.01 * spread_u
    rate_long = 0.25 / LENGTH * jnp.exp(math.log(16.0) * spread_u)
    by_kind = jnp.where(kinds == 0, rate_fast, jnp.where(kinds == 1, rate_slow, rate_tone))
    rates = jnp.where(lasting, rate_long, by_kind)
    level_u = jax.random.uniform(jax.random.fold_in(key, 14), (CHANNELS, MODES), jnp.float32)
    weight_abs = jnp.where(lasting, 0.05 + 0.05 * level_u, 0.15 + 0.2 * level_u)
    signs = jnp.where(jax.random.bernoulli(jax.random.fold_in(key, 15), 0.5, (CHANNELS, MODES)), 1.0, -1.0)
    residues = signs * weight_abs * jnp.sqrt(1.0 - jnp.exp(-2.0 * rates))
    return (rates.astype(jnp.float32), residues.astype(jnp.float32))


def draw_decay_rate(key, part):
    return mode_table(key)[0]


def draw_residue(key, part):
    return mode_table(key)[1]


def draw_skip_gain(key, part):
    level_u = jax.random.uniform(jax.random.fold_in(key, 16), (CHANNELS,), jnp.float32)
    return (0.15 * (2.0 * level_u - 1.0)).astype(jnp.float32)


def draw_signal(key, part):
    values = jnp.clip(jax.random.normal(jax.random.fold_in(key, 31), (CHANNELS, LENGTH), jnp.float32), -6.0, 6.0)
    return values.astype(jnp.bfloat16)


def draw_inner_gate(key, part):
    values = jnp.clip(jax.random.normal(jax.random.fold_in(key, 41), (CHANNELS, LENGTH), jnp.float32), -6.0, 6.0)
    return values.astype(jnp.bfloat16)


def steps_of(key, shape, split, smallest, high):
    def one(axis_at, blocks):
        steps = jax.random.uniform(jax.random.fold_in(jax.random.fold_in(key, 6), axis_at), (blocks,), jnp.float32, smallest / len(split), high / len(split))
        return jnp.repeat(jnp.exp(steps), shape[axis_at] // blocks).reshape((-1,) + (1,) * (len(shape) - axis_at - 1))

    gain = one(*split[0])
    for cut in split[1:]:
        gain = gain * one(*cut)
    return gain


def scatter_about(rng, shape, spread, limit, pieces=(), kind=jnp.bfloat16):
    gain = steps_of(rng, shape, pieces, -0.22, 0.18) if pieces else 1.0
    entries = jax.random.normal(rng, shape, jnp.float32) * spread * gain
    return jnp.minimum(jnp.maximum(entries, -limit), limit).astype(kind)


def setup_inputs(seed: int = 0) -> dict:
    splits = jax.random.split(jax.random.key(seed), 7)
    signal = draw_signal(jax.random.fold_in(splits[6], 71), 0)
    inner_gate = draw_inner_gate(jax.random.fold_in(splits[6], 71), 0)
    outer_gate = scatter_about(splits[2], (CHANNELS, LENGTH), 1.0, 6.0, ((1, 32),))
    decay_rate = draw_decay_rate(jax.random.fold_in(splits[6], 71), 0)
    residue = draw_residue(jax.random.fold_in(splits[6], 71), 0)
    skip_gain = draw_skip_gain(jax.random.fold_in(splits[6], 71), 0)
    return {"signal": signal, "inner_gate": inner_gate, "outer_gate": outer_gate, "decay_rate": decay_rate, "residue": residue, "skip_gain": skip_gain}


def conv_block(packed):
    drive_blk, rate_blk, residue_blk = packed
    length = drive_blk.shape[1]
    offsets = jnp.arange(length).astype(drive_blk.dtype)
    kernel = jnp.zeros_like(drive_blk)
    for mode_idx in range(rate_blk.shape[1]):
        kernel = kernel + residue_blk[:, mode_idx:mode_idx + 1] * jnp.exp(-rate_blk[:, mode_idx:mode_idx + 1] * offsets[None, :])
    spectrum = jnp.fft.rfft(drive_blk, n=2 * length) * jnp.fft.rfft(kernel, n=2 * length)
    return jnp.fft.irfft(spectrum, n=2 * length)[:, :length]


def reference(signal, inner_gate, outer_gate, decay_rate, residue, skip_gain):
    gated_in = (inner_gate.astype(jnp.float32) * signal.astype(jnp.float32)).astype(jnp.bfloat16)
    driven = lax.optimization_barrier(gated_in).astype(jnp.float32)
    group_size = min(64, CHANNELS)
    groups = CHANNELS // group_size
    convolved = lax.map(conv_block, (driven.reshape(groups, group_size, LENGTH), decay_rate.reshape(groups, group_size, MODES), residue.reshape(groups, group_size, MODES)))
    convolved = convolved.reshape(CHANNELS, LENGTH)
    offsets = jnp.arange(LENGTH).astype(jnp.float32)

    def mode_state(mode_idx):
        rate_col = lax.dynamic_slice_in_dim(decay_rate, mode_idx, 1, 1)
        return jnp.sum(driven * jnp.exp(-rate_col * (LENGTH - 1.0 - offsets)[None, :]), axis=1)

    states = lax.map(mode_state, jnp.arange(MODES, dtype=jnp.int32))
    modal_state = residue * states.T
    layer_out = (outer_gate.astype(jnp.float32) * (convolved + skip_gain[:, None] * driven)).astype(jnp.bfloat16)
    return layer_out, modal_state
```

```python
import jax
import jax.numpy as jnp
from jax import lax
from jax.sharding import PartitionSpec as P


def prefix_matrix(length):
    rows = lax.iota(jnp.int32, length)
    return (rows[:, None] <= rows[None, :]).astype(jnp.bfloat16)


def prefix_sum(values, tri):
    upper = values.astype(jnp.bfloat16)
    lower = (values - upper.astype(jnp.float32)).astype(jnp.bfloat16)
    first = jnp.einsum("mcs,st->mct", upper, tri, preferred_element_type=jnp.float32)
    second = jnp.einsum("mcs,st->mct", lower, tri, preferred_element_type=jnp.float32)
    return first + second


def on_device(signal, inner_gate, outer_gate, decay_rate, residue, skip_gain):
    channels, tok_block = signal.shape
    seq_count = lax.axis_size("seq")
    chan_count = lax.axis_size("chan")
    blocks = seq_count * chan_count
    owner_idx = lax.axis_index("seq") * chan_count + lax.axis_index("chan")
    gated_in = (inner_gate.astype(jnp.float32) * signal.astype(jnp.float32)).astype(jnp.bfloat16)
    driven = lax.optimization_barrier(gated_in).astype(jnp.float32)
    rate_t = decay_rate.T
    residue_t = residue.T
    offsets = jnp.arange(tok_block, dtype=jnp.float32)
    rising = jnp.exp(rate_t[:, :, None] * offsets[None, None, :])
    falling = jnp.exp(-rate_t[:, :, None] * offsets[None, None, :])
    running = prefix_sum(rising * driven[None, :, :], prefix_matrix(tok_block))
    block_state = running[:, :, tok_block - 1] * falling[:, :, tok_block - 1]
    gathered = lax.all_gather(block_state, ("seq", "chan"), axis=0, tiled=False)
    source = jnp.arange(blocks, dtype=jnp.int32)
    lag = jnp.maximum(owner_idx - 1 - source, 0).astype(jnp.float32)
    carry_w = jnp.exp(-rate_t[None] * (tok_block * lag)[:, None, None])
    carry_w = jnp.where((source < owner_idx)[:, None, None], carry_w, 0.0)
    carry_in = jnp.sum(carry_w * gathered, axis=0)
    tail_lag = (blocks - 1 - source).astype(jnp.float32)
    tail_w = jnp.exp(-rate_t[None] * (tok_block * tail_lag)[:, None, None])
    final_state = jnp.sum(tail_w * gathered, axis=0)
    modal_state = residue * final_state.T
    local_part = jnp.sum(residue_t[:, :, None] * falling * running, axis=0)
    carry_coef = residue_t * jnp.exp(-rate_t) * carry_in
    carry_part = jnp.sum(carry_coef[:, :, None] * falling, axis=0)
    convolved = local_part + carry_part
    layer_out = (outer_gate.astype(jnp.float32) * (convolved + skip_gain[:, None] * driven)).astype(
        jnp.bfloat16
    )
    return (layer_out, modal_state)


def solution(mesh):
    placed = (
        P(None, ("seq", "chan")),
        P(None, ("seq", "chan")),
        P(None, ("seq", "chan")),
        P(),
        P(),
        P(),
    )
    return jax.shard_map(
        on_device,
        mesh=mesh,
        in_specs=placed,
        out_specs=(P(None, ("seq", "chan")), P()),
        check_vma=False,
    )
```

```python
import jax
import jax.numpy as jnp
from jax import lax
from jax.sharding import PartitionSpec as P


def prefix_matrix(length):
    rows = lax.iota(jnp.int32, length)
    return (rows[:, None] <= rows[None, :]).astype(jnp.bfloat16)


def prefix_sum(values, tri):
    upper = values.astype(jnp.bfloat16)
    lower = (values - upper.astype(jnp.float32)).astype(jnp.bfloat16)
    first = jnp.einsum("mcs,st->mct", upper, tri, preferred_element_type=jnp.float32)
    second = jnp.einsum("mcs,st->mct", lower, tri, preferred_element_type=jnp.float32)
    return first + second


def on_device(signal, inner_gate, outer_gate, decay_rate, residue, skip_gain):
    channels, tok_block = signal.shape
    seq_count = lax.axis_size("seq")
    chan_count = lax.axis_size("chan")
    blocks = seq_count * chan_count
    owner_idx = lax.axis_index("seq") * chan_count + lax.axis_index("chan")
    gated_in = (inner_gate.astype(jnp.float32) * signal.astype(jnp.float32)).astype(jnp.bfloat16)
    driven = lax.optimization_barrier(gated_in).astype(jnp.float32)
    rate_t = decay_rate.T
    residue_t = residue.T
    offsets = jnp.arange(tok_block, dtype=jnp.float32)
    rising = jnp.exp(rate_t[:, :, None] * offsets[None, None, :])
    falling = jnp.exp(-rate_t[:, :, None] * offsets[None, None, :])
    running = prefix_sum(rising * driven[None, :, :], prefix_matrix(tok_block))
    to_end = jnp.exp(-rate_t[:, :, None] * (tok_block - 1.0 - offsets)[None, None, :])
    block_state = jnp.sum(to_end * driven[None, :, :], axis=2)
    rounds = blocks.bit_length() - 1
    assert 1 << rounds == blocks
    span_rate = rate_t * tok_block
    carry_in = jnp.zeros_like(block_state)
    group_total = block_state
    for level in range(rounds):
        width = 1 << level
        pairs = [(src_i, src_i ^ width) for src_i in range(blocks)]
        other = lax.ppermute(group_total, ("seq", "chan"), pairs)
        upper = (owner_idx & width) != 0
        place = (owner_idx % width).astype(jnp.float32)
        carry_in = jnp.where(upper, carry_in + jnp.exp(-span_rate * place) * other, carry_in)
        later = jnp.where(upper, group_total, other)
        earlier = jnp.where(upper, other, group_total)
        group_total = later + jnp.exp(-span_rate * width) * earlier
    modal_state = residue * group_total.T
    local_part = jnp.sum(residue_t[:, :, None] * falling * running, axis=0)
    carry_coef = residue_t * jnp.exp(-rate_t) * carry_in
    carry_part = jnp.sum(carry_coef[:, :, None] * falling, axis=0)
    convolved = local_part + carry_part
    layer_out = (outer_gate.astype(jnp.float32) * (convolved + skip_gain[:, None] * driven)).astype(
        jnp.bfloat16
    )
    return (layer_out, modal_state)


def solution(mesh):
    placed = (
        P(None, ("seq", "chan")),
        P(None, ("seq", "chan")),
        P(None, ("seq", "chan")),
        P(),
        P(),
        P(),
    )
    return jax.shard_map(
        on_device,
        mesh=mesh,
        in_specs=placed,
        out_specs=(P(None, ("seq", "chan")), P()),
        check_vma=False,
    )
```

```python
import jax
import jax.numpy as jnp
from jax import lax
from jax.sharding import PartitionSpec as P


def prefix_matrix(length):
    rows = lax.iota(jnp.int32, length)
    return (rows[:, None] <= rows[None, :]).astype(jnp.bfloat16)


def prefix_sum(values, tri):
    upper = values.astype(jnp.bfloat16)
    lower = (values - upper.astype(jnp.float32)).astype(jnp.bfloat16)
    first = jnp.einsum("mcs,st->mct", upper, tri, preferred_element_type=jnp.float32)
    second = jnp.einsum("mcs,st->mct", lower, tri, preferred_element_type=jnp.float32)
    return first + second


def local_chunk(driven, rate_t, residue_t, skip_gain):
    tok_block = driven.shape[1]
    offsets = jnp.arange(tok_block, dtype=jnp.float32)
    rising = jnp.exp(rate_t[:, :, None] * offsets[None, None, :])
    falling = jnp.exp(-rate_t[:, :, None] * offsets[None, None, :])
    running = prefix_sum(rising * driven[None, :, :], prefix_matrix(tok_block))
    local_part = jnp.sum(residue_t[:, :, None] * falling * running, axis=0)
    return local_part + skip_gain[:, None] * driven


def on_device(signal, inner_gate, outer_gate, decay_rate, residue, skip_gain):
    channels, tok_block = signal.shape
    seq_count = lax.axis_size("seq")
    chan_count = lax.axis_size("chan")
    blocks = seq_count * chan_count
    owner_idx = lax.axis_index("seq") * chan_count + lax.axis_index("chan")
    gated_in = (inner_gate.astype(jnp.float32) * signal.astype(jnp.float32)).astype(jnp.bfloat16)
    driven = lax.optimization_barrier(gated_in).astype(jnp.float32)
    rate_t = decay_rate.T
    residue_t = residue.T
    offsets = jnp.arange(tok_block, dtype=jnp.float32)
    to_end = jnp.exp(-rate_t[:, :, None] * (tok_block - 1.0 - offsets)[None, None, :])
    block_state = jnp.sum(to_end * driven[None, :, :], axis=2)
    rounds = blocks.bit_length() - 1
    assert 1 << rounds == blocks
    pieces = min(rounds, 4)
    piece = channels // pieces
    span_rate = rate_t * tok_block
    carry_in = jnp.zeros_like(block_state)
    group_total = block_state
    direct = []
    for level in range(rounds):
        width = 1 << level
        if level < pieces:
            lo = level * piece
            group_total, chunk_in = lax.optimization_barrier((group_total, driven[lo:lo + piece]))
        pairs = [(src_i, src_i ^ width) for src_i in range(blocks)]
        other = lax.ppermute(group_total, ("seq", "chan"), pairs)
        if level < pieces:
            chunk_out = local_chunk(
                chunk_in, rate_t[:, lo:lo + piece], residue_t[:, lo:lo + piece], skip_gain[lo:lo + piece]
            )
        upper = (owner_idx & width) != 0
        place = (owner_idx % width).astype(jnp.float32)
        carry_in = jnp.where(upper, carry_in + jnp.exp(-span_rate * place) * other, carry_in)
        later = jnp.where(upper, group_total, other)
        earlier = jnp.where(upper, other, group_total)
        group_total = later + jnp.exp(-span_rate * width) * earlier
        if level < pieces:
            group_total, carry_in, chunk_out = lax.optimization_barrier((group_total, carry_in, chunk_out))
            direct.append(chunk_out)
    modal_state = residue * group_total.T
    falling = jnp.exp(-rate_t[:, :, None] * offsets[None, None, :])
    carry_coef = residue_t * jnp.exp(-rate_t) * carry_in
    carry_part = jnp.sum(carry_coef[:, :, None] * falling, axis=0)
    convolved = jnp.concatenate(direct, axis=0) + carry_part
    layer_out = (outer_gate.astype(jnp.float32) * convolved).astype(jnp.bfloat16)
    return (layer_out, modal_state)


def solution(mesh):
    placed = (
        P(None, ("seq", "chan")),
        P(None, ("seq", "chan")),
        P(None, ("seq", "chan")),
        P(),
        P(),
        P(),
    )
    return jax.shard_map(
        on_device,
        mesh=mesh,
        in_specs=placed,
        out_specs=(P(None, ("seq", "chan")), P()),
        check_vma=False,
    )
```

```python
import jax
import jax.numpy as jnp
from jax import lax
from jax.sharding import PartitionSpec as P


def prefix_matrix(length):
    rows = lax.iota(jnp.int32, length)
    return (rows[:, None] <= rows[None, :]).astype(jnp.bfloat16)


def prefix_sum(values, tri):
    upper = values.astype(jnp.bfloat16)
    lower = (values - upper.astype(jnp.float32)).astype(jnp.bfloat16)
    first = jnp.einsum("mcs,st->mct", upper, tri, preferred_element_type=jnp.float32)
    second = jnp.einsum("mcs,st->mct", lower, tri, preferred_element_type=jnp.float32)
    return first + second


def local_chunk(driven, rate_t, residue_t, skip_gain):
    tok_block = driven.shape[1]
    offsets = jnp.arange(tok_block, dtype=jnp.float32)
    rising = jnp.exp(rate_t[:, :, None] * offsets[None, None, :])
    falling = jnp.exp(-rate_t[:, :, None] * offsets[None, None, :])
    running = prefix_sum(rising * driven[None, :, :], prefix_matrix(tok_block))
    local_part = jnp.sum(residue_t[:, :, None] * falling * running, axis=0)
    return local_part + skip_gain[:, None] * driven


def chunk_bounds(channels, pieces):
    return [min(channels, (channels * i // pieces + 7) // 8 * 8) for i in range(pieces + 1)]


def level_sizes(blocks):
    rounds = blocks.bit_length() - 1
    assert 1 << rounds == blocks
    sizes = [4] * (rounds // 2)
    if rounds % 2:
        sizes.append(2)
    return sizes


def on_device(signal, inner_gate, outer_gate, decay_rate, residue, skip_gain):
    channels, tok_block = signal.shape
    seq_count = lax.axis_size("seq")
    chan_count = lax.axis_size("chan")
    blocks = seq_count * chan_count
    owner_idx = lax.axis_index("seq") * chan_count + lax.axis_index("chan")
    gated_in = (inner_gate.astype(jnp.float32) * signal.astype(jnp.float32)).astype(jnp.bfloat16)
    driven = lax.optimization_barrier(gated_in).astype(jnp.float32)
    rate_t = decay_rate.T
    residue_t = residue.T
    offsets = jnp.arange(tok_block, dtype=jnp.float32)
    to_end = jnp.exp(-rate_t[:, :, None] * (tok_block - 1.0 - offsets)[None, None, :])
    block_state = jnp.sum(to_end * driven[None, :, :], axis=2)
    sizes = level_sizes(blocks)
    bounds = chunk_bounds(channels, len(sizes))
    span_rate = rate_t * tok_block
    carry_in = jnp.zeros_like(block_state)
    group_total = block_state
    direct = []
    width = 1
    for level, radix in enumerate(sizes):
        lo, hi = bounds[level], bounds[level + 1]
        group_total, chunk_in = lax.optimization_barrier((group_total, driven[lo:hi]))
        span = width * radix
        received = [group_total]
        for shift in range(1, radix):
            pairs = [
                (src_i, src_i - src_i % span + ((src_i // width + shift) % radix) * width + src_i % width)
                for src_i in range(blocks)
            ]
            received.append(lax.ppermute(group_total, ("seq", "chan"), pairs))
        chunk_out = local_chunk(chunk_in, rate_t[:, lo:hi], residue_t[:, lo:hi], skip_gain[lo:hi])
        stacked = jnp.stack(received)
        place = owner_idx // width % radix
        inner = (owner_idx % width).astype(jnp.float32)
        new_total = jnp.zeros_like(group_total)
        for part in range(radix):
            value = lax.dynamic_index_in_dim(stacked, (place - part) % radix, 0, keepdims=False)
            gap = jnp.maximum(place - 1 - part, 0).astype(jnp.float32) * width + inner
            weight = jnp.where(part < place, jnp.exp(-span_rate * gap), 0.0)
            carry_in = carry_in + weight * value
            new_total = new_total + jnp.exp(-span_rate * ((radix - 1 - part) * width)) * value
        group_total = new_total
        group_total, carry_in, chunk_out = lax.optimization_barrier((group_total, carry_in, chunk_out))
        direct.append(chunk_out)
        width = span
    modal_state = residue * group_total.T
    falling = jnp.exp(-rate_t[:, :, None] * offsets[None, None, :])
    carry_coef = residue_t * jnp.exp(-rate_t) * carry_in
    carry_part = jnp.sum(carry_coef[:, :, None] * falling, axis=0)
    convolved = jnp.concatenate(direct, axis=0) + carry_part
    layer_out = (outer_gate.astype(jnp.float32) * convolved).astype(jnp.bfloat16)
    return (layer_out, modal_state)


def solution(mesh):
    placed = (
        P(None, ("seq", "chan")),
        P(None, ("seq", "chan")),
        P(None, ("seq", "chan")),
        P(),
        P(),
        P(),
    )
    return jax.shard_map(
        on_device,
        mesh=mesh,
        in_specs=placed,
        out_specs=(P(None, ("seq", "chan")), P()),
        check_vma=False,
    )
```

```python
import jax
import jax.numpy as jnp
from jax import lax
from jax.sharding import PartitionSpec as P


def prefix_matrix(length):
    rows = lax.iota(jnp.int32, length)
    return (rows[:, None] <= rows[None, :]).astype(jnp.bfloat16)


def prefix_sum(values, tri):
    upper = values.astype(jnp.bfloat16)
    lower = (values - upper.astype(jnp.float32)).astype(jnp.bfloat16)
    first = jnp.einsum("mcs,st->mct", upper, tri, preferred_element_type=jnp.float32)
    second = jnp.einsum("mcs,st->mct", lower, tri, preferred_element_type=jnp.float32)
    return first + second


def local_chunk(driven, rate_t, residue_t, skip_gain):
    tok_block = driven.shape[1]
    offsets = jnp.arange(tok_block, dtype=jnp.float32)
    rising = jnp.exp(rate_t[:, :, None] * offsets[None, None, :])
    falling = jnp.exp(-rate_t[:, :, None] * offsets[None, None, :])
    running = prefix_sum(rising * driven[None, :, :], prefix_matrix(tok_block))
    local_part = jnp.sum(residue_t[:, :, None] * falling * running, axis=0)
    return local_part + skip_gain[:, None] * driven


def on_device(signal, inner_gate, outer_gate, decay_rate, residue, skip_gain):
    channels, tok_block = signal.shape
    seq_count = lax.axis_size("seq")
    chan_count = lax.axis_size("chan")
    blocks = seq_count * chan_count
    owner_idx = lax.axis_index("seq") * chan_count + lax.axis_index("chan")
    gated_in = (inner_gate.astype(jnp.float32) * signal.astype(jnp.float32)).astype(jnp.bfloat16)
    driven = lax.optimization_barrier(gated_in).astype(jnp.float32)
    rate_t = decay_rate.T
    residue_t = residue.T
    offsets = jnp.arange(tok_block, dtype=jnp.float32)
    half = tok_block // 2
    folded = driven[None, :, :half] * jnp.exp(-rate_t * half)[:, :, None] + driven[None, :, half:]
    to_end = jnp.exp(-rate_t[:, :, None] * (half - 1.0 - offsets[:half])[None, None, :])
    block_state = jnp.sum(to_end * folded, axis=2)
    rounds = blocks.bit_length() - 1
    assert 1 << rounds == blocks
    pieces = min(rounds, 4)
    piece = channels // pieces
    span_rate = rate_t * tok_block
    carry_in = jnp.zeros_like(block_state)
    group_total = block_state
    direct = []
    for level in range(rounds):
        width = 1 << level
        if level < pieces:
            lo = level * piece
            group_total, chunk_in = lax.optimization_barrier((group_total, driven[lo:lo + piece]))
        pairs = [(src_i, src_i ^ width) for src_i in range(blocks)]
        other = lax.ppermute(group_total, ("seq", "chan"), pairs)
        if level < pieces:
            chunk_out = local_chunk(
                chunk_in, rate_t[:, lo:lo + piece], residue_t[:, lo:lo + piece], skip_gain[lo:lo + piece]
            )
        upper = (owner_idx & width) != 0
        place = (owner_idx % width).astype(jnp.float32)
        carry_in = jnp.where(upper, carry_in + jnp.exp(-span_rate * place) * other, carry_in)
        later = jnp.where(upper, group_total, other)
        earlier = jnp.where(upper, other, group_total)
        group_total = later + jnp.exp(-span_rate * width) * earlier
        if level < pieces:
            group_total, carry_in, chunk_out = lax.optimization_barrier((group_total, carry_in, chunk_out))
            direct.append(chunk_out)
    modal_state = residue * group_total.T
    carry_coef = residue_t * jnp.exp(-rate_t) * carry_in
    convolved = jnp.concatenate(direct, axis=0)
    for mode in range(rate_t.shape[0]):
        falling = jnp.exp(-rate_t[mode][:, None] * offsets[None, :])
        convolved = convolved + carry_coef[mode][:, None] * falling
    layer_out = (outer_gate.astype(jnp.float32) * convolved).astype(jnp.bfloat16)
    return (layer_out, modal_state)


def solution(mesh):
    placed = (
        P(None, ("seq", "chan")),
        P(None, ("seq", "chan")),
        P(None, ("seq", "chan")),
        P(),
        P(),
        P(),
    )
    return jax.shard_map(
        on_device,
        mesh=mesh,
        in_specs=placed,
        out_specs=(P(None, ("seq", "chan")), P()),
        check_vma=False,
    )
```

```python
import jax
import jax.numpy as jnp
from jax import lax
from jax.sharding import PartitionSpec as P


def prefix_matrix(length):
    rows = lax.iota(jnp.int32, length)
    return (rows[:, None] <= rows[None, :]).astype(jnp.bfloat16)


def prefix_sum(values, tri):
    upper = values.astype(jnp.bfloat16)
    lower = (values - upper.astype(jnp.float32)).astype(jnp.bfloat16)
    first = jnp.einsum("mcs,st->mct", upper, tri, preferred_element_type=jnp.float32)
    second = jnp.einsum("mcs,st->mct", lower, tri, preferred_element_type=jnp.float32)
    return first + second


def local_chunk(driven, rate_t, residue_t, skip_gain):
    tok_block = driven.shape[1]
    offsets = jnp.arange(tok_block, dtype=jnp.float32)
    rising = jnp.exp(rate_t[:, :, None] * offsets[None, None, :])
    falling = jnp.exp(-rate_t[:, :, None] * offsets[None, None, :])
    running = prefix_sum(rising * driven[None, :, :], prefix_matrix(tok_block))
    local_part = jnp.sum(residue_t[:, :, None] * falling * running, axis=0)
    return local_part + skip_gain[:, None] * driven


def on_device(signal, inner_gate, outer_gate, decay_rate, residue, skip_gain):
    channels, tok_block = signal.shape
    seq_count = lax.axis_size("seq")
    chan_count = lax.axis_size("chan")
    blocks = seq_count * chan_count
    owner_idx = lax.axis_index("seq") * chan_count + lax.axis_index("chan")
    gated_in = (inner_gate.astype(jnp.float32) * signal.astype(jnp.float32)).astype(jnp.bfloat16)
    driven = lax.optimization_barrier(gated_in).astype(jnp.float32)
    rate_t = decay_rate.T
    residue_t = residue.T
    offsets = jnp.arange(tok_block, dtype=jnp.float32)
    half = tok_block // 2
    half_span = jnp.exp(-rate_t * half)[:, :, None]
    near_end = jnp.exp(-rate_t[:, :, None] * (half - 1.0 - offsets[:half])[None, None, :])
    to_end = jnp.concatenate([near_end * half_span, near_end], axis=2)
    block_state = jnp.sum(to_end * driven[None, :, :], axis=2)
    rounds = blocks.bit_length() - 1
    assert 1 << rounds == blocks
    pieces = min(rounds, 4)
    piece = channels // pieces
    span_rate = rate_t * tok_block
    carry_in = jnp.zeros_like(block_state)
    group_total = block_state
    direct = []
    for level in range(rounds):
        width = 1 << level
        if level < pieces:
            lo = level * piece
            group_total, chunk_in = lax.optimization_barrier((group_total, driven[lo:lo + piece]))
        pairs = [(src_i, src_i ^ width) for src_i in range(blocks)]
        other = lax.ppermute(group_total, ("seq", "chan"), pairs)
        if level < pieces:
            chunk_out = local_chunk(
                chunk_in, rate_t[:, lo:lo + piece], residue_t[:, lo:lo + piece], skip_gain[lo:lo + piece]
            )
        upper = (owner_idx & width) != 0
        place = (owner_idx % width).astype(jnp.float32)
        carry_in = jnp.where(upper, carry_in + jnp.exp(-span_rate * place) * other, carry_in)
        later = jnp.where(upper, group_total, other)
        earlier = jnp.where(upper, other, group_total)
        group_total = later + jnp.exp(-span_rate * width) * earlier
        if level < pieces:
            group_total, carry_in, chunk_out = lax.optimization_barrier((group_total, carry_in, chunk_out))
            direct.append(chunk_out)
    modal_state = residue * group_total.T
    near_start = jnp.exp(-rate_t[:, :, None] * offsets[None, None, :half])
    carry_coef = (residue_t * jnp.exp(-rate_t) * carry_in)[:, :, None]
    carry_part = jnp.concatenate(
        [jnp.sum(carry_coef * near_start, axis=0), jnp.sum(carry_coef * half_span * near_start, axis=0)], axis=1
    )
    convolved = jnp.concatenate(direct, axis=0) + carry_part
    layer_out = (outer_gate.astype(jnp.float32) * convolved).astype(jnp.bfloat16)
    return (layer_out, modal_state)


def solution(mesh):
    placed = (
        P(None, ("seq", "chan")),
        P(None, ("seq", "chan")),
        P(None, ("seq", "chan")),
        P(),
        P(),
        P(),
    )
    return jax.shard_map(
        on_device,
        mesh=mesh,
        in_specs=placed,
        out_specs=(P(None, ("seq", "chan")), P()),
        check_vma=False,
    )
```

```python
import jax
import jax.numpy as jnp
from jax import lax
from jax.experimental import pallas as pl
from jax.experimental.pallas import tpu as pltpu
from jax.sharding import PartitionSpec as P


def prefix_matrix(length):
    rows = lax.iota(jnp.int32, length)
    return (rows[:, None] <= rows[None, :]).astype(jnp.bfloat16)


def prefix_sum(values, tri):
    upper = values.astype(jnp.bfloat16)
    lower = (values - upper.astype(jnp.float32)).astype(jnp.bfloat16)
    first = jnp.einsum("mcs,st->mct", upper, tri, preferred_element_type=jnp.float32)
    second = jnp.einsum("mcs,st->mct", lower, tri, preferred_element_type=jnp.float32)
    return first + second


def local_chunk(driven, rate_t, residue_t, skip_gain):
    tok_block = driven.shape[1]
    offsets = jnp.arange(tok_block, dtype=jnp.float32)
    rising = jnp.exp(rate_t[:, :, None] * offsets[None, None, :])
    falling = jnp.exp(-rate_t[:, :, None] * offsets[None, None, :])
    running = prefix_sum(rising * driven[None, :, :], prefix_matrix(tok_block))
    local_part = jnp.sum(residue_t[:, :, None] * falling * running, axis=0)
    return local_part + skip_gain[:, None] * driven


def finish_kernel(*refs):
    coef_ref, rate_ref, total_ref, residue_ref, outer_ref = refs[:5]
    direct_refs = refs[5:-2]
    out_ref, modal_ref = refs[-2:]
    piece, tok_block = direct_refs[0].shape
    modes = coef_ref.shape[0]
    half = tok_block // 2
    lanes = lax.broadcasted_iota(jnp.int32, (1, half), 1).astype(jnp.float32)
    for index, direct_ref in enumerate(direct_refs):
        rows = slice(index * piece, (index + 1) * piece)
        coef = coef_ref[:, rows].T
        rate = rate_ref[:, rows].T
        modal_ref[rows, :] = residue_ref[rows, :] * total_ref[:, rows].T
        low = direct_ref[:, :half]
        high = direct_ref[:, half:]
        for mode in range(modes):
            rate_m = rate[:, mode:mode + 1]
            coef_m = coef[:, mode:mode + 1]
            power = jnp.exp(-rate_m * lanes)
            low = low + coef_m * power
            high = high + (coef_m * jnp.exp(-rate_m * half)) * power
        out_ref[rows, :half] = (outer_ref[rows, :half].astype(jnp.float32) * low).astype(out_ref.dtype)
        out_ref[rows, half:] = (outer_ref[rows, half:].astype(jnp.float32) * high).astype(out_ref.dtype)


def finish(carry_coef, rate_t, group_total, residue, outer_gate, direct):
    channels, tok_block = outer_gate.shape
    modes = rate_t.shape[0]
    whole = pl.BlockSpec(memory_space=pltpu.VMEM)
    return pl.pallas_call(
        finish_kernel,
        out_shape=(
            jax.ShapeDtypeStruct((channels, tok_block), jnp.bfloat16),
            jax.ShapeDtypeStruct((channels, modes), jnp.float32),
        ),
        in_specs=[whole] * (5 + len(direct)),
        out_specs=(whole, whole),
        cost_estimate=pl.CostEstimate(
            flops=4 * modes * channels * tok_block,
            transcendentals=modes * channels * tok_block // 2,
            bytes_accessed=10 * channels * tok_block,
        ),
    )(carry_coef, rate_t, group_total, residue, outer_gate, *direct)


def on_device(signal, inner_gate, outer_gate, decay_rate, residue, skip_gain):
    channels, tok_block = signal.shape
    seq_count = lax.axis_size("seq")
    chan_count = lax.axis_size("chan")
    blocks = seq_count * chan_count
    owner_idx = lax.axis_index("seq") * chan_count + lax.axis_index("chan")
    gated_in = (inner_gate.astype(jnp.float32) * signal.astype(jnp.float32)).astype(jnp.bfloat16)
    driven = lax.optimization_barrier(gated_in).astype(jnp.float32)
    rate_t = decay_rate.T
    residue_t = residue.T
    offsets = jnp.arange(tok_block, dtype=jnp.float32)
    to_end = jnp.exp(-rate_t[:, :, None] * (tok_block - 1.0 - offsets)[None, None, :])
    block_state = jnp.sum(to_end * driven[None, :, :], axis=2)
    rounds = blocks.bit_length() - 1
    assert 1 << rounds == blocks
    pieces = min(rounds, 4)
    piece = channels // pieces
    span_rate = rate_t * tok_block
    carry_in = jnp.zeros_like(block_state)
    group_total = block_state
    direct = []
    for level in range(rounds):
        width = 1 << level
        if level < pieces:
            lo = level * piece
            group_total, chunk_in = lax.optimization_barrier((group_total, driven[lo:lo + piece]))
        pairs = [(src_i, src_i ^ width) for src_i in range(blocks)]
        other = lax.ppermute(group_total, ("seq", "chan"), pairs)
        if level < pieces:
            chunk_out = local_chunk(
                chunk_in, rate_t[:, lo:lo + piece], residue_t[:, lo:lo + piece], skip_gain[lo:lo + piece]
            )
        upper = (owner_idx & width) != 0
        place = (owner_idx % width).astype(jnp.float32)
        carry_in = jnp.where(upper, carry_in + jnp.exp(-span_rate * place) * other, carry_in)
        later = jnp.where(upper, group_total, other)
        earlier = jnp.where(upper, other, group_total)
        group_total = later + jnp.exp(-span_rate * width) * earlier
        if level < pieces:
            group_total, carry_in, chunk_out = lax.optimization_barrier((group_total, carry_in, chunk_out))
            direct.append(chunk_out)
    carry_coef = residue_t * jnp.exp(-rate_t) * carry_in
    layer_out, modal_state = finish(carry_coef, rate_t, group_total, residue, outer_gate, direct)
    return (layer_out, modal_state)


def solution(mesh):
    placed = (
        P(None, ("seq", "chan")),
        P(None, ("seq", "chan")),
        P(None, ("seq", "chan")),
        P(),
        P(),
        P(),
    )
    return jax.shard_map(
        on_device,
        mesh=mesh,
        in_specs=placed,
        out_specs=(P(None, ("seq", "chan")), P()),
        check_vma=False,
    )
```

```python
import jax
import jax.numpy as jnp
from jax import lax
from jax.sharding import PartitionSpec as P


def prefix_matrix(length):
    rows = lax.iota(jnp.int32, length)
    return (rows[:, None] <= rows[None, :]).astype(jnp.bfloat16)


def prefix_sum(values, tri):
    upper = values.astype(jnp.bfloat16)
    lower = (values - upper.astype(jnp.float32)).astype(jnp.bfloat16)
    first = jnp.einsum("mcs,st->mct", upper, tri, preferred_element_type=jnp.float32)
    second = jnp.einsum("mcs,st->mct", lower, tri, preferred_element_type=jnp.float32)
    return first + second


def local_chunk(driven, rate_t, residue_t, skip_gain):
    tok_block = driven.shape[1]
    offsets = jnp.arange(tok_block, dtype=jnp.float32)
    rising = jnp.exp(rate_t[:, :, None] * offsets[None, None, :])
    falling = jnp.exp(-rate_t[:, :, None] * offsets[None, None, :])
    running = prefix_sum(rising * driven[None, :, :], prefix_matrix(tok_block))
    local_part = jnp.sum(residue_t[:, :, None] * falling * running, axis=0)
    return local_part + skip_gain[:, None] * driven


def on_device(signal, inner_gate, outer_gate, decay_rate, residue, skip_gain):
    channels, tok_block = signal.shape
    seq_count = lax.axis_size("seq")
    chan_count = lax.axis_size("chan")
    blocks = seq_count * chan_count
    owner_idx = lax.axis_index("seq") * chan_count + lax.axis_index("chan")
    gated_in = (inner_gate.astype(jnp.float32) * signal.astype(jnp.float32)).astype(jnp.bfloat16)
    driven = gated_in.astype(jnp.float32)
    rate_t = decay_rate.T
    residue_t = residue.T
    offsets = jnp.arange(tok_block, dtype=jnp.float32)
    to_end = jnp.exp(-rate_t[:, :, None] * (tok_block - 1.0 - offsets)[None, None, :])
    block_state = jnp.sum(to_end * driven[None, :, :], axis=2)
    rounds = blocks.bit_length() - 1
    assert 1 << rounds == blocks
    pieces = min(rounds, 4)
    piece = channels // pieces
    span_rate = rate_t * tok_block
    carry_in = jnp.zeros_like(block_state)
    group_total = block_state
    direct = []
    for level in range(rounds):
        width = 1 << level
        if level < pieces:
            lo = level * piece
            group_total, chunk_in = lax.optimization_barrier((group_total, driven[lo:lo + piece]))
        pairs = [(src_i, src_i ^ width) for src_i in range(blocks)]
        other = lax.ppermute(group_total, ("seq", "chan"), pairs)
        if level < pieces:
            chunk_out = local_chunk(
                chunk_in, rate_t[:, lo:lo + piece], residue_t[:, lo:lo + piece], skip_gain[lo:lo + piece]
            )
        upper = (owner_idx & width) != 0
        place = (owner_idx % width).astype(jnp.float32)
        carry_in = jnp.where(upper, carry_in + jnp.exp(-span_rate * place) * other, carry_in)
        later = jnp.where(upper, group_total, other)
        earlier = jnp.where(upper, other, group_total)
        group_total = later + jnp.exp(-span_rate * width) * earlier
        if level < pieces:
            group_total, carry_in, chunk_out = lax.optimization_barrier((group_total, carry_in, chunk_out))
            direct.append(chunk_out)
    modal_state = residue * group_total.T
    falling = jnp.exp(-rate_t[:, :, None] * offsets[None, None, :])
    carry_coef = residue_t * jnp.exp(-rate_t) * carry_in
    carry_part = jnp.sum(carry_coef[:, :, None] * falling, axis=0)
    convolved = jnp.concatenate(direct, axis=0) + carry_part
    layer_out = (outer_gate.astype(jnp.float32) * convolved).astype(jnp.bfloat16)
    return (layer_out, modal_state)


def solution(mesh):
    placed = (
        P(None, ("seq", "chan")),
        P(None, ("seq", "chan")),
        P(None, ("seq", "chan")),
        P(),
        P(),
        P(),
    )
    return jax.shard_map(
        on_device,
        mesh=mesh,
        in_specs=placed,
        out_specs=(P(None, ("seq", "chan")), P()),
        check_vma=False,
    )
```

```python
import jax
import jax.numpy as jnp
from jax import lax
from jax.sharding import PartitionSpec as P


def prefix_matrix(length):
    rows = lax.iota(jnp.int32, length)
    return (rows[:, None] <= rows[None, :]).astype(jnp.bfloat16)


def prefix_sum(values, tri):
    upper = values.astype(jnp.bfloat16)
    lower = (values - upper.astype(jnp.float32)).astype(jnp.bfloat16)
    first = jnp.einsum("mcs,st->mct", upper, tri, preferred_element_type=jnp.float32)
    second = jnp.einsum("mcs,st->mct", lower, tri, preferred_element_type=jnp.float32)
    return first + second


def local_chunk(driven, rate_t, residue_t, skip_gain):
    tok_block = driven.shape[1]
    offsets = jnp.arange(tok_block, dtype=jnp.float32)
    rising = jnp.exp(rate_t[:, :, None] * offsets[None, None, :])
    falling = jnp.exp(-rate_t[:, :, None] * offsets[None, None, :])
    running = prefix_sum(rising * driven[None, :, :], prefix_matrix(tok_block))
    local_part = jnp.sum(residue_t[:, :, None] * falling * running, axis=0)
    return local_part + skip_gain[:, None] * driven


def on_device(signal, inner_gate, outer_gate, decay_rate, residue, skip_gain):
    channels, tok_block = signal.shape
    seq_count = lax.axis_size("seq")
    chan_count = lax.axis_size("chan")
    blocks = seq_count * chan_count
    owner_idx = lax.axis_index("seq") * chan_count + lax.axis_index("chan")
    gated_in = (inner_gate.astype(jnp.float32) * signal.astype(jnp.float32)).astype(jnp.bfloat16)
    driven = lax.optimization_barrier(gated_in).astype(jnp.float32)
    rate_t = decay_rate.T
    residue_t = residue.T
    offsets = jnp.arange(tok_block, dtype=jnp.float32)
    to_end = jnp.exp(-rate_t[:, :, None] * (tok_block - 1.0 - offsets)[None, None, :])
    block_state = jnp.sum(to_end * driven[None, :, :], axis=2)
    rounds = blocks.bit_length() - 1
    assert 1 << rounds == blocks
    pieces = rounds
    bounds = [min(channels, (channels * i // pieces + 7) // 8 * 8) for i in range(pieces + 1)]
    span_rate = rate_t * tok_block
    carry_in = jnp.zeros_like(block_state)
    group_total = block_state
    direct = []
    for level in range(rounds):
        width = 1 << level
        if level < pieces:
            lo, hi = bounds[level], bounds[level + 1]
            group_total, chunk_in = lax.optimization_barrier((group_total, driven[lo:hi]))
        pairs = [(src_i, src_i ^ width) for src_i in range(blocks)]
        other = lax.ppermute(group_total, ("seq", "chan"), pairs)
        if level < pieces:
            chunk_out = local_chunk(
                chunk_in, rate_t[:, lo:hi], residue_t[:, lo:hi], skip_gain[lo:hi]
            )
        upper = (owner_idx & width) != 0
        place = (owner_idx % width).astype(jnp.float32)
        carry_in = jnp.where(upper, carry_in + jnp.exp(-span_rate * place) * other, carry_in)
        later = jnp.where(upper, group_total, other)
        earlier = jnp.where(upper, other, group_total)
        group_total = later + jnp.exp(-span_rate * width) * earlier
        if level < pieces:
            group_total, carry_in, chunk_out = lax.optimization_barrier((group_total, carry_in, chunk_out))
            direct.append(chunk_out)
    modal_state = residue * group_total.T
    falling = jnp.exp(-rate_t[:, :, None] * offsets[None, None, :])
    carry_coef = residue_t * jnp.exp(-rate_t) * carry_in
    carry_part = jnp.sum(carry_coef[:, :, None] * falling, axis=0)
    convolved = jnp.concatenate(direct, axis=0) + carry_part
    layer_out = (outer_gate.astype(jnp.float32) * convolved).astype(jnp.bfloat16)
    return (layer_out, modal_state)


def solution(mesh):
    placed = (
        P(None, ("seq", "chan")),
        P(None, ("seq", "chan")),
        P(None, ("seq", "chan")),
        P(),
        P(),
        P(),
    )
    return jax.shard_map(
        on_device,
        mesh=mesh,
        in_specs=placed,
        out_specs=(P(None, ("seq", "chan")), P()),
        check_vma=False,
    )
```

```python
import jax
import jax.numpy as jnp
from jax import lax
from jax.sharding import PartitionSpec as P


def prefix_matrix(length):
    rows = lax.iota(jnp.int32, length)
    return (rows[:, None] <= rows[None, :]).astype(jnp.bfloat16)


def prefix_sum(values, tri):
    upper = values.astype(jnp.bfloat16)
    lower = (values - upper.astype(jnp.float32)).astype(jnp.bfloat16)
    first = jnp.einsum("mcs,st->mct", upper, tri, preferred_element_type=jnp.float32)
    second = jnp.einsum("mcs,st->mct", lower, tri, preferred_element_type=jnp.float32)
    return first + second


def gate(signal, inner_gate):
    product = inner_gate.astype(jnp.float32) * signal.astype(jnp.float32)
    return lax.reduce_precision(product, exponent_bits=8, mantissa_bits=7)


def local_chunk(driven, rate_t, residue_t, skip_gain):
    tok_block = driven.shape[1]
    offsets = jnp.arange(tok_block, dtype=jnp.float32)
    rising = jnp.exp(rate_t[:, :, None] * offsets[None, None, :])
    falling = jnp.exp(-rate_t[:, :, None] * offsets[None, None, :])
    running = prefix_sum(rising * driven[None, :, :], prefix_matrix(tok_block))
    local_part = jnp.sum(residue_t[:, :, None] * falling * running, axis=0)
    return local_part + skip_gain[:, None] * driven


def on_device(signal, inner_gate, outer_gate, decay_rate, residue, skip_gain):
    channels, tok_block = signal.shape
    seq_count = lax.axis_size("seq")
    chan_count = lax.axis_size("chan")
    blocks = seq_count * chan_count
    owner_idx = lax.axis_index("seq") * chan_count + lax.axis_index("chan")
    driven = gate(signal, inner_gate)
    rate_t = decay_rate.T
    residue_t = residue.T
    offsets = jnp.arange(tok_block, dtype=jnp.float32)
    to_end = jnp.exp(-rate_t[:, :, None] * (tok_block - 1.0 - offsets)[None, None, :])
    block_state = jnp.sum(to_end * driven[None, :, :], axis=2)
    rounds = blocks.bit_length() - 1
    assert 1 << rounds == blocks
    pieces = min(rounds, 4)
    piece = channels // pieces
    span_rate = rate_t * tok_block
    carry_in = jnp.zeros_like(block_state)
    group_total = block_state
    direct = []
    for level in range(rounds):
        width = 1 << level
        if level < pieces:
            lo = level * piece
            group_total, sig_in, inner_in = lax.optimization_barrier(
                (group_total, signal[lo:lo + piece], inner_gate[lo:lo + piece])
            )
            chunk_in = gate(sig_in, inner_in)
        pairs = [(src_i, src_i ^ width) for src_i in range(blocks)]
        other = lax.ppermute(group_total, ("seq", "chan"), pairs)
        if level < pieces:
            chunk_out = local_chunk(
                chunk_in, rate_t[:, lo:lo + piece], residue_t[:, lo:lo + piece], skip_gain[lo:lo + piece]
            )
        upper = (owner_idx & width) != 0
        place = (owner_idx % width).astype(jnp.float32)
        carry_in = jnp.where(upper, carry_in + jnp.exp(-span_rate * place) * other, carry_in)
        later = jnp.where(upper, group_total, other)
        earlier = jnp.where(upper, other, group_total)
        group_total = later + jnp.exp(-span_rate * width) * earlier
        if level < pieces:
            group_total, carry_in, chunk_out = lax.optimization_barrier((group_total, carry_in, chunk_out))
            direct.append(chunk_out)
    modal_state = residue * group_total.T
    falling = jnp.exp(-rate_t[:, :, None] * offsets[None, None, :])
    carry_coef = residue_t * jnp.exp(-rate_t) * carry_in
    carry_part = jnp.sum(carry_coef[:, :, None] * falling, axis=0)
    convolved = jnp.concatenate(direct, axis=0) + carry_part
    layer_out = (outer_gate.astype(jnp.float32) * convolved).astype(jnp.bfloat16)
    return (layer_out, modal_state)


def solution(mesh):
    placed = (
        P(None, ("seq", "chan")),
        P(None, ("seq", "chan")),
        P(None, ("seq", "chan")),
        P(),
        P(),
        P(),
    )
    return jax.shard_map(
        on_device,
        mesh=mesh,
        in_specs=placed,
        out_specs=(P(None, ("seq", "chan")), P()),
        check_vma=False,
    )
```

```python
import jax
import jax.numpy as jnp
from jax import lax
from jax.sharding import PartitionSpec as P


def prefix_matrix(length):
    rows = lax.iota(jnp.int32, length)
    return (rows[:, None] <= rows[None, :]).astype(jnp.bfloat16)


def prefix_sum(values, tri):
    upper = values.astype(jnp.bfloat16)
    lower = (values - upper.astype(jnp.float32)).astype(jnp.bfloat16)
    first = jnp.einsum("mcs,st->mct", upper, tri, preferred_element_type=jnp.float32)
    second = jnp.einsum("mcs,st->mct", lower, tri, preferred_element_type=jnp.float32)
    return first + second


def power_table(rate_t, first, step):
    modes, channels = rate_t.shape
    coarse = jnp.arange(16, dtype=jnp.float32) * (16.0 * step)
    fine = first + jnp.arange(16, dtype=jnp.float32) * step
    high = jnp.exp(-rate_t[:, :, None] * coarse[None, None, :])
    low = jnp.exp(-rate_t[:, :, None] * fine[None, None, :])
    return (high[:, :, :, None] * low[:, :, None, :]).reshape(modes, channels, 256)


def local_chunk(driven, rate_t, residue_t, skip_gain):
    tok_block = driven.shape[1]
    offsets = jnp.arange(tok_block, dtype=jnp.float32)
    rising = jnp.exp(rate_t[:, :, None] * offsets[None, None, :])
    falling = jnp.exp(-rate_t[:, :, None] * offsets[None, None, :])
    running = prefix_sum(rising * driven[None, :, :], prefix_matrix(tok_block))
    local_part = jnp.sum(residue_t[:, :, None] * falling * running, axis=0)
    return local_part + skip_gain[:, None] * driven


def on_device(signal, inner_gate, outer_gate, decay_rate, residue, skip_gain):
    channels, tok_block = signal.shape
    seq_count = lax.axis_size("seq")
    chan_count = lax.axis_size("chan")
    blocks = seq_count * chan_count
    owner_idx = lax.axis_index("seq") * chan_count + lax.axis_index("chan")
    gated_in = (inner_gate.astype(jnp.float32) * signal.astype(jnp.float32)).astype(jnp.bfloat16)
    driven = lax.optimization_barrier(gated_in).astype(jnp.float32)
    rate_t = decay_rate.T
    residue_t = residue.T
    offsets = jnp.arange(tok_block, dtype=jnp.float32)
    to_end = power_table(rate_t, tok_block - 1.0, -1.0)
    block_state = jnp.sum(to_end * driven[None, :, :], axis=2)
    rounds = blocks.bit_length() - 1
    assert 1 << rounds == blocks
    pieces = min(rounds, 4)
    piece = channels // pieces
    span_rate = rate_t * tok_block
    carry_in = jnp.zeros_like(block_state)
    group_total = block_state
    direct = []
    for level in range(rounds):
        width = 1 << level
        if level < pieces:
            lo = level * piece
            group_total, chunk_in = lax.optimization_barrier((group_total, driven[lo:lo + piece]))
        pairs = [(src_i, src_i ^ width) for src_i in range(blocks)]
        other = lax.ppermute(group_total, ("seq", "chan"), pairs)
        if level < pieces:
            chunk_out = local_chunk(
                chunk_in, rate_t[:, lo:lo + piece], residue_t[:, lo:lo + piece], skip_gain[lo:lo + piece]
            )
        upper = (owner_idx & width) != 0
        place = (owner_idx % width).astype(jnp.float32)
        carry_in = jnp.where(upper, carry_in + jnp.exp(-span_rate * place) * other, carry_in)
        later = jnp.where(upper, group_total, other)
        earlier = jnp.where(upper, other, group_total)
        group_total = later + jnp.exp(-span_rate * width) * earlier
        if level < pieces:
            group_total, carry_in, chunk_out = lax.optimization_barrier((group_total, carry_in, chunk_out))
            direct.append(chunk_out)
    modal_state = residue * group_total.T
    falling = power_table(rate_t, 0.0, 1.0)
    carry_coef = residue_t * jnp.exp(-rate_t) * carry_in
    carry_part = jnp.sum(carry_coef[:, :, None] * falling, axis=0)
    convolved = jnp.concatenate(direct, axis=0) + carry_part
    layer_out = (outer_gate.astype(jnp.float32) * convolved).astype(jnp.bfloat16)
    return (layer_out, modal_state)


def solution(mesh):
    placed = (
        P(None, ("seq", "chan")),
        P(None, ("seq", "chan")),
        P(None, ("seq", "chan")),
        P(),
        P(),
        P(),
    )
    return jax.shard_map(
        on_device,
        mesh=mesh,
        in_specs=placed,
        out_specs=(P(None, ("seq", "chan")), P()),
        check_vma=False,
    )
```

```python
import jax
import jax.numpy as jnp
from jax import lax
from jax.sharding import PartitionSpec as P


def prefix_matrix(length):
    rows = lax.iota(jnp.int32, length)
    return (rows[:, None] <= rows[None, :]).astype(jnp.bfloat16)


def prefix_sum(values, tri):
    upper = values.astype(jnp.bfloat16)
    lower = (values - upper.astype(jnp.float32)).astype(jnp.bfloat16)
    first = jnp.einsum("mcs,st->mct", upper, tri, preferred_element_type=jnp.float32)
    second = jnp.einsum("mcs,st->mct", lower, tri, preferred_element_type=jnp.float32)
    return first + second


def power_table(rate_t, first, step):
    modes, channels = rate_t.shape
    coarse = jnp.arange(16, dtype=jnp.float32) * (16.0 * step)
    fine = first + jnp.arange(16, dtype=jnp.float32) * step
    high = jnp.exp(-rate_t[:, :, None] * coarse[None, None, :])
    low = jnp.exp(-rate_t[:, :, None] * fine[None, None, :])
    return (high[:, :, :, None] * low[:, :, None, :]).reshape(modes, channels, 256)


def local_chunk(driven, rate_t, residue_t, skip_gain):
    tok_block = driven.shape[1]
    offsets = jnp.arange(tok_block, dtype=jnp.float32)
    rising = jnp.exp(rate_t[:, :, None] * offsets[None, None, :])
    falling = jnp.exp(-rate_t[:, :, None] * offsets[None, None, :])
    running = prefix_sum(rising * driven[None, :, :], prefix_matrix(tok_block))
    local_part = jnp.sum(residue_t[:, :, None] * falling * running, axis=0)
    return local_part + skip_gain[:, None] * driven


def on_device(signal, inner_gate, outer_gate, decay_rate, residue, skip_gain):
    channels, tok_block = signal.shape
    seq_count = lax.axis_size("seq")
    chan_count = lax.axis_size("chan")
    blocks = seq_count * chan_count
    owner_idx = lax.axis_index("seq") * chan_count + lax.axis_index("chan")
    gated_in = (inner_gate.astype(jnp.float32) * signal.astype(jnp.float32)).astype(jnp.bfloat16)
    driven = lax.optimization_barrier(gated_in).astype(jnp.float32)
    rate_t = decay_rate.T
    residue_t = residue.T
    offsets = jnp.arange(tok_block, dtype=jnp.float32)
    to_end = power_table(rate_t, tok_block - 1.0, -1.0)
    block_state = jnp.sum(to_end * driven[None, :, :], axis=2)
    rounds = blocks.bit_length() - 1
    assert 1 << rounds == blocks
    pieces = min(rounds, 4)
    piece = channels // pieces
    span_rate = rate_t * tok_block
    carry_in = jnp.zeros_like(block_state)
    group_total = block_state
    direct = []
    for level in range(rounds):
        width = 1 << level
        if level < pieces:
            lo = level * piece
            group_total, chunk_in = lax.optimization_barrier((group_total, driven[lo:lo + piece]))
        pairs = [(src_i, src_i ^ width) for src_i in range(blocks)]
        other = lax.ppermute(group_total, ("seq", "chan"), pairs)
        if level < pieces:
            chunk_out = local_chunk(
                chunk_in, rate_t[:, lo:lo + piece], residue_t[:, lo:lo + piece], skip_gain[lo:lo + piece]
            )
        upper = (owner_idx & width) != 0
        place = (owner_idx % width).astype(jnp.float32)
        carry_in = jnp.where(upper, carry_in + jnp.exp(-span_rate * place) * other, carry_in)
        shrink = jnp.exp(-span_rate * width)
        if level == rounds - 1:
            own_w = residue_t * jnp.where(upper, 1.0, shrink)
            other_w = residue_t * jnp.where(upper, shrink, 1.0)
            own_part, other_w = lax.optimization_barrier((own_w * group_total, other_w))
            modal_t = own_part + other_w * other
        later = jnp.where(upper, group_total, other)
        earlier = jnp.where(upper, other, group_total)
        group_total = later + shrink * earlier
        if level < pieces:
            group_total, carry_in, chunk_out = lax.optimization_barrier((group_total, carry_in, chunk_out))
            direct.append(chunk_out)
    modal_state = modal_t.T
    falling = power_table(rate_t, 0.0, 1.0)
    carry_coef = residue_t * jnp.exp(-rate_t) * carry_in
    carry_part = jnp.sum(carry_coef[:, :, None] * falling, axis=0)
    convolved = jnp.concatenate(direct, axis=0) + carry_part
    layer_out = (outer_gate.astype(jnp.float32) * convolved).astype(jnp.bfloat16)
    return (layer_out, modal_state)


def solution(mesh):
    placed = (
        P(None, ("seq", "chan")),
        P(None, ("seq", "chan")),
        P(None, ("seq", "chan")),
        P(),
        P(),
        P(),
    )
    return jax.shard_map(
        on_device,
        mesh=mesh,
        in_specs=placed,
        out_specs=(P(None, ("seq", "chan")), P()),
        check_vma=False,
    )
```

```python
import jax
import jax.numpy as jnp
from jax import lax
from jax.sharding import PartitionSpec as P


def prefix_matrix(length):
    rows = lax.iota(jnp.int32, length)
    return (rows[:, None] <= rows[None, :]).astype(jnp.bfloat16)


def prefix_sum(values, tri):
    upper = values.astype(jnp.bfloat16)
    lower = (values - upper.astype(jnp.float32)).astype(jnp.bfloat16)
    first = jnp.einsum("mcs,st->mct", upper, tri, preferred_element_type=jnp.float32)
    second = jnp.einsum("mcs,st->mct", lower, tri, preferred_element_type=jnp.float32)
    return first + second


def power_factors(rate_t, first, step):
    coarse = jnp.arange(16, dtype=jnp.float32) * (16.0 * step)
    fine = first + jnp.arange(16, dtype=jnp.float32) * step
    high = jnp.exp(-rate_t[:, :, None] * coarse[None, None, :])
    low = jnp.exp(-rate_t[:, :, None] * fine[None, None, :])
    return high, low


def outer_table(high, low):
    modes, channels = high.shape[:2]
    return (high[:, :, :, None] * low[:, :, None, :]).reshape(modes, channels, 256)


def power_table(rate_t, first, step):
    return outer_table(*power_factors(rate_t, first, step))


def local_chunk(driven, rate_t, residue_t, skip_gain):
    tok_block = driven.shape[1]
    offsets = jnp.arange(tok_block, dtype=jnp.float32)
    rising = jnp.exp(rate_t[:, :, None] * offsets[None, None, :])
    falling = jnp.exp(-rate_t[:, :, None] * offsets[None, None, :])
    running = prefix_sum(rising * driven[None, :, :], prefix_matrix(tok_block))
    local_part = jnp.sum(residue_t[:, :, None] * falling * running, axis=0)
    return local_part + skip_gain[:, None] * driven


def on_device(signal, inner_gate, outer_gate, decay_rate, residue, skip_gain):
    channels, tok_block = signal.shape
    seq_count = lax.axis_size("seq")
    chan_count = lax.axis_size("chan")
    blocks = seq_count * chan_count
    owner_idx = lax.axis_index("seq") * chan_count + lax.axis_index("chan")
    state_high, state_low = power_factors(decay_rate.T, tok_block - 1.0, -1.0)
    state_high, state_low, signal, inner_gate = lax.optimization_barrier(
        (state_high, state_low, signal, inner_gate)
    )
    gated_in = (inner_gate.astype(jnp.float32) * signal.astype(jnp.float32)).astype(jnp.bfloat16)
    driven = lax.optimization_barrier(gated_in).astype(jnp.float32)
    rate_t = decay_rate.T
    residue_t = residue.T
    offsets = jnp.arange(tok_block, dtype=jnp.float32)
    to_end = outer_table(state_high, state_low)
    block_state = jnp.sum(to_end * driven[None, :, :], axis=2)
    rounds = blocks.bit_length() - 1
    assert 1 << rounds == blocks
    pieces = min(rounds, 4)
    piece = channels // pieces
    span_rate = rate_t * tok_block
    carry_in = jnp.zeros_like(block_state)
    group_total = block_state
    direct = []
    for level in range(rounds):
        width = 1 << level
        if level < pieces:
            lo = level * piece
            group_total, chunk_in = lax.optimization_barrier((group_total, driven[lo:lo + piece]))
        pairs = [(src_i, src_i ^ width) for src_i in range(blocks)]
        other = lax.ppermute(group_total, ("seq", "chan"), pairs)
        if level < pieces:
            chunk_out = local_chunk(
                chunk_in, rate_t[:, lo:lo + piece], residue_t[:, lo:lo + piece], skip_gain[lo:lo + piece]
            )
        upper = (owner_idx & width) != 0
        place = (owner_idx % width).astype(jnp.float32)
        carry_in = jnp.where(upper, carry_in + jnp.exp(-span_rate * place) * other, carry_in)
        shrink = jnp.exp(-span_rate * width)
        if level == rounds - 1:
            own_w = residue_t * jnp.where(upper, 1.0, shrink)
            other_w = residue_t * jnp.where(upper, shrink, 1.0)
            own_part, other_w = lax.optimization_barrier((own_w * group_total, other_w))
            modal_t = own_part + other_w * other
        later = jnp.where(upper, group_total, other)
        earlier = jnp.where(upper, other, group_total)
        group_total = later + shrink * earlier
        if level < pieces:
            group_total, carry_in, chunk_out = lax.optimization_barrier((group_total, carry_in, chunk_out))
            direct.append(chunk_out)
    modal_state = modal_t.T
    falling = power_table(rate_t, 0.0, 1.0)
    carry_coef = residue_t * jnp.exp(-rate_t) * carry_in
    carry_part = jnp.sum(carry_coef[:, :, None] * falling, axis=0)
    convolved = jnp.concatenate(direct, axis=0) + carry_part
    layer_out = (outer_gate.astype(jnp.float32) * convolved).astype(jnp.bfloat16)
    return (layer_out, modal_state)


def solution(mesh):
    placed = (
        P(None, ("seq", "chan")),
        P(None, ("seq", "chan")),
        P(None, ("seq", "chan")),
        P(),
        P(),
        P(),
    )
    return jax.shard_map(
        on_device,
        mesh=mesh,
        in_specs=placed,
        out_specs=(P(None, ("seq", "chan")), P()),
        check_vma=False,
    )
```

```python
import jax
import jax.numpy as jnp
from jax import lax
from jax.sharding import PartitionSpec as P


def prefix_matrix(length):
    rows = lax.iota(jnp.int32, length)
    return (rows[:, None] <= rows[None, :]).astype(jnp.bfloat16)


def prefix_sum(values, tri):
    upper = values.astype(jnp.bfloat16)
    lower = (values - upper.astype(jnp.float32)).astype(jnp.bfloat16)
    first = jnp.einsum("mcs,st->mct", upper, tri, preferred_element_type=jnp.float32)
    second = jnp.einsum("mcs,st->mct", lower, tri, preferred_element_type=jnp.float32)
    return first + second


def power_factors(rate_t, first, step):
    coarse = jnp.arange(16, dtype=jnp.float32) * (16.0 * step)
    fine = first + jnp.arange(16, dtype=jnp.float32) * step
    high = jnp.exp(-rate_t[:, :, None] * coarse[None, None, :])
    low = jnp.exp(-rate_t[:, :, None] * fine[None, None, :])
    return high, low


def outer_table(high, low):
    modes, channels = high.shape[:2]
    return (high[:, :, :, None] * low[:, :, None, :]).reshape(modes, channels, 256)


def power_table(rate_t, first, step):
    return outer_table(*power_factors(rate_t, first, step))


def local_chunk(driven, rate_t, residue_t, skip_gain):
    tok_block = driven.shape[1]
    offsets = jnp.arange(tok_block, dtype=jnp.float32)
    rising = jnp.exp(rate_t[:, :, None] * offsets[None, None, :])
    falling = jnp.exp(-rate_t[:, :, None] * offsets[None, None, :])
    running = prefix_sum(rising * driven[None, :, :], prefix_matrix(tok_block))
    local_part = jnp.sum(residue_t[:, :, None] * falling * running, axis=0)
    return local_part + skip_gain[:, None] * driven


def on_device(signal, inner_gate, outer_gate, decay_rate, residue, skip_gain):
    channels, tok_block = signal.shape
    seq_count = lax.axis_size("seq")
    chan_count = lax.axis_size("chan")
    blocks = seq_count * chan_count
    owner_idx = lax.axis_index("seq") * chan_count + lax.axis_index("chan")
    state_high, state_low = power_factors(decay_rate.T, tok_block - 1.0, -1.0)
    state_high, state_low, signal, inner_gate = lax.optimization_barrier(
        (state_high, state_low, signal, inner_gate)
    )
    gated_in = (inner_gate.astype(jnp.float32) * signal.astype(jnp.float32)).astype(jnp.bfloat16)
    driven = lax.optimization_barrier(gated_in).astype(jnp.float32)
    rate_t = decay_rate.T
    residue_t = residue.T
    offsets = jnp.arange(tok_block, dtype=jnp.float32)
    to_end = outer_table(state_high, state_low)
    block_state = jnp.sum(to_end * driven[None, :, :], axis=2)
    rounds = blocks.bit_length() - 1
    assert 1 << rounds == blocks
    on_chip = chan_count.bit_length() - 1
    chunk_levels = [level for level in range(rounds) if level != on_chip][:4]
    pieces = len(chunk_levels)
    piece = channels // pieces
    span_rate = rate_t * tok_block
    carry_in = jnp.zeros_like(block_state)
    group_total = block_state
    direct = []
    for level in range(rounds):
        width = 1 << level
        if level in chunk_levels:
            lo = chunk_levels.index(level) * piece
            group_total, chunk_in = lax.optimization_barrier((group_total, driven[lo:lo + piece]))
        pairs = [(src_i, src_i ^ width) for src_i in range(blocks)]
        other = lax.ppermute(group_total, ("seq", "chan"), pairs)
        if level in chunk_levels:
            chunk_out = local_chunk(
                chunk_in, rate_t[:, lo:lo + piece], residue_t[:, lo:lo + piece], skip_gain[lo:lo + piece]
            )
        upper = (owner_idx & width) != 0
        place = (owner_idx % width).astype(jnp.float32)
        carry_in = jnp.where(upper, carry_in + jnp.exp(-span_rate * place) * other, carry_in)
        shrink = jnp.exp(-span_rate * width)
        if level == rounds - 1:
            own_w = residue_t * jnp.where(upper, 1.0, shrink)
            other_w = residue_t * jnp.where(upper, shrink, 1.0)
            own_part, other_w = lax.optimization_barrier((own_w * group_total, other_w))
            modal_t = own_part + other_w * other
        later = jnp.where(upper, group_total, other)
        earlier = jnp.where(upper, other, group_total)
        group_total = later + shrink * earlier
        if level in chunk_levels:
            group_total, carry_in, chunk_out = lax.optimization_barrier((group_total, carry_in, chunk_out))
            direct.append(chunk_out)
    modal_state = modal_t.T
    falling = power_table(rate_t, 0.0, 1.0)
    carry_coef = residue_t * jnp.exp(-rate_t) * carry_in
    carry_part = jnp.sum(carry_coef[:, :, None] * falling, axis=0)
    convolved = jnp.concatenate(direct, axis=0) + carry_part
    layer_out = (outer_gate.astype(jnp.float32) * convolved).astype(jnp.bfloat16)
    return (layer_out, modal_state)


def solution(mesh):
    placed = (
        P(None, ("seq", "chan")),
        P(None, ("seq", "chan")),
        P(None, ("seq", "chan")),
        P(),
        P(),
        P(),
    )
    return jax.shard_map(
        on_device,
        mesh=mesh,
        in_specs=placed,
        out_specs=(P(None, ("seq", "chan")), P()),
        check_vma=False,
    )
```

```python
import jax
import jax.numpy as jnp
from jax import lax
from jax.sharding import PartitionSpec as P


def prefix_matrix(length):
    rows = lax.iota(jnp.int32, length)
    return (rows[:, None] <= rows[None, :]).astype(jnp.bfloat16)


def prefix_sum(values, tri):
    upper = values.astype(jnp.bfloat16)
    lower = (values - upper.astype(jnp.float32)).astype(jnp.bfloat16)
    first = jnp.einsum("mcs,st->mct", upper, tri, preferred_element_type=jnp.float32)
    second = jnp.einsum("mcs,st->mct", lower, tri, preferred_element_type=jnp.float32)
    return first + second


def power_factors(rate_t, first, step):
    coarse = jnp.arange(16, dtype=jnp.float32) * (16.0 * step)
    fine = first + jnp.arange(16, dtype=jnp.float32) * step
    high = jnp.exp(-rate_t[:, :, None] * coarse[None, None, :])
    low = jnp.exp(-rate_t[:, :, None] * fine[None, None, :])
    return high, low


def outer_table(high, low):
    modes, channels = high.shape[:2]
    return (high[:, :, :, None] * low[:, :, None, :]).reshape(modes, channels, 256)


def power_table(rate_t, first, step):
    return outer_table(*power_factors(rate_t, first, step))


def lane_factors(rate_t, first, step, length):
    fine_n = 1 << (length.bit_length() // 2)
    coarse_n = length // fine_n
    assert coarse_n * fine_n == length
    coarse = jnp.arange(coarse_n, dtype=jnp.float32) * (fine_n * step)
    fine = first + jnp.arange(fine_n, dtype=jnp.float32) * step
    high = jnp.exp(-rate_t[:, None, :] * coarse[None, :, None])
    low = jnp.exp(-rate_t[:, None, :] * fine[None, :, None])
    return high, low


def local_chunk(driven, rate_t, residue_t, skip_gain):
    tok_block = driven.shape[1]
    offsets = jnp.arange(tok_block, dtype=jnp.float32)
    rising = jnp.exp(rate_t[:, :, None] * offsets[None, None, :])
    falling = jnp.exp(-rate_t[:, :, None] * offsets[None, None, :])
    running = prefix_sum(rising * driven[None, :, :], prefix_matrix(tok_block))
    local_part = jnp.sum(residue_t[:, :, None] * falling * running, axis=0)
    return local_part + skip_gain[:, None] * driven


def on_device(signal, inner_gate, outer_gate, decay_rate, residue, skip_gain):
    channels, tok_block = signal.shape
    seq_count = lax.axis_size("seq")
    chan_count = lax.axis_size("chan")
    blocks = seq_count * chan_count
    owner_idx = lax.axis_index("seq") * chan_count + lax.axis_index("chan")
    state_high, state_low = lane_factors(decay_rate.T, tok_block - 1.0, -1.0, tok_block)
    state_high, state_low, signal, inner_gate = lax.optimization_barrier(
        (state_high, state_low, signal, inner_gate)
    )
    gated_in = (inner_gate.astype(jnp.float32) * signal.astype(jnp.float32)).astype(jnp.bfloat16)
    driven = lax.optimization_barrier(gated_in).astype(jnp.float32)
    rate_t = decay_rate.T
    residue_t = residue.T
    offsets = jnp.arange(tok_block, dtype=jnp.float32)
    coarse_n, fine_n = state_high.shape[1], state_low.shape[1]
    driven_t = driven.T.reshape(coarse_n, fine_n, channels)
    partial = jnp.sum(state_low[:, None, :, :] * driven_t[None, :, :, :], axis=2)
    block_state = jnp.sum(state_high * partial, axis=1)
    rounds = blocks.bit_length() - 1
    assert 1 << rounds == blocks
    on_chip = chan_count.bit_length() - 1
    chunk_levels = [level for level in range(rounds) if level != on_chip][:4]
    pieces = len(chunk_levels)
    piece = channels // pieces
    span_rate = rate_t * tok_block
    carry_in = jnp.zeros_like(block_state)
    group_total = block_state
    direct = []
    for level in range(rounds):
        width = 1 << level
        if level in chunk_levels:
            lo = chunk_levels.index(level) * piece
            group_total, chunk_in = lax.optimization_barrier((group_total, driven[lo:lo + piece]))
        pairs = [(src_i, src_i ^ width) for src_i in range(blocks)]
        other = lax.ppermute(group_total, ("seq", "chan"), pairs)
        if level in chunk_levels:
            chunk_out = local_chunk(
                chunk_in, rate_t[:, lo:lo + piece], residue_t[:, lo:lo + piece], skip_gain[lo:lo + piece]
            )
        upper = (owner_idx & width) != 0
        place = (owner_idx % width).astype(jnp.float32)
        carry_in = jnp.where(upper, carry_in + jnp.exp(-span_rate * place) * other, carry_in)
        shrink = jnp.exp(-span_rate * width)
        if level == rounds - 1:
            own_w = residue_t * jnp.where(upper, 1.0, shrink)
            other_w = residue_t * jnp.where(upper, shrink, 1.0)
            own_part, other_w = lax.optimization_barrier((own_w * group_total, other_w))
            modal_t = own_part + other_w * other
        later = jnp.where(upper, group_total, other)
        earlier = jnp.where(upper, other, group_total)
        group_total = later + shrink * earlier
        if level in chunk_levels:
            group_total, carry_in, chunk_out = lax.optimization_barrier((group_total, carry_in, chunk_out))
            direct.append(chunk_out)
    modal_state = modal_t.T
    carry_coef = residue_t * jnp.exp(-rate_t) * carry_in
    carry_high, carry_low = lane_factors(rate_t, 0.0, 1.0, tok_block)
    carry_high = carry_coef[:, None, :] * carry_high
    carry_t = jnp.sum(carry_high[:, :, None, :] * carry_low[:, None, :, :], axis=0)
    carry_part = carry_t.reshape(tok_block, channels).T
    convolved = jnp.concatenate(direct, axis=0) + carry_part
    layer_out = (outer_gate.astype(jnp.float32) * convolved).astype(jnp.bfloat16)
    return (layer_out, modal_state)


def solution(mesh):
    placed = (
        P(None, ("seq", "chan")),
        P(None, ("seq", "chan")),
        P(None, ("seq", "chan")),
        P(),
        P(),
        P(),
    )
    return jax.shard_map(
        on_device,
        mesh=mesh,
        in_specs=placed,
        out_specs=(P(None, ("seq", "chan")), P()),
        check_vma=False,
    )
```

```python
import jax
import jax.numpy as jnp
from jax import lax
from jax.sharding import PartitionSpec as P


def prefix_matrix(length):
    rows = lax.iota(jnp.int32, length)
    return (rows[:, None] <= rows[None, :]).astype(jnp.bfloat16)


def prefix_sum(values, tri):
    upper = values.astype(jnp.bfloat16)
    lower = (values - upper.astype(jnp.float32)).astype(jnp.bfloat16)
    first = jnp.einsum("mcs,st->mct", upper, tri, preferred_element_type=jnp.float32)
    second = jnp.einsum("mcs,st->mct", lower, tri, preferred_element_type=jnp.float32)
    return first + second


def power_factors(rate_t, first, step):
    coarse = jnp.arange(16, dtype=jnp.float32) * (16.0 * step)
    fine = first + jnp.arange(16, dtype=jnp.float32) * step
    high = jnp.exp(-rate_t[:, :, None] * coarse[None, None, :])
    low = jnp.exp(-rate_t[:, :, None] * fine[None, None, :])
    return high, low


def outer_table(high, low):
    modes, channels = high.shape[:2]
    return (high[:, :, :, None] * low[:, :, None, :]).reshape(modes, channels, 256)


def power_table(rate_t, first, step):
    return outer_table(*power_factors(rate_t, first, step))


def lane_factors(rate_t, first, step, length):
    fine_n = 1 << (length.bit_length() // 2)
    coarse_n = length // fine_n
    assert coarse_n * fine_n == length
    coarse = jnp.arange(coarse_n, dtype=jnp.float32) * (fine_n * step)
    fine = first + jnp.arange(fine_n, dtype=jnp.float32) * step
    high = jnp.exp(-rate_t[:, None, :] * coarse[None, :, None])
    low = jnp.exp(-rate_t[:, None, :] * fine[None, :, None])
    return high, low


def local_chunk(driven, rate_t, residue_t, skip_gain):
    tok_block = driven.shape[1]
    offsets = jnp.arange(tok_block, dtype=jnp.float32)
    rising = jnp.exp(rate_t[:, :, None] * offsets[None, None, :])
    falling = jnp.exp(-rate_t[:, :, None] * offsets[None, None, :])
    running = prefix_sum(rising * driven[None, :, :], prefix_matrix(tok_block))
    local_part = jnp.sum(residue_t[:, :, None] * falling * running, axis=0)
    return local_part + skip_gain[:, None] * driven


def on_device(signal, inner_gate, outer_gate, decay_rate, residue, skip_gain):
    channels, tok_block = signal.shape
    seq_count = lax.axis_size("seq")
    chan_count = lax.axis_size("chan")
    blocks = seq_count * chan_count
    owner_idx = lax.axis_index("seq") * chan_count + lax.axis_index("chan")
    state_high, state_low = power_factors(decay_rate.T, tok_block - 1.0, -1.0)
    state_high, state_low, signal, inner_gate = lax.optimization_barrier(
        (state_high, state_low, signal, inner_gate)
    )
    gated_in = (inner_gate.astype(jnp.float32) * signal.astype(jnp.float32)).astype(jnp.bfloat16)
    driven = lax.optimization_barrier(gated_in).astype(jnp.float32)
    rate_t = decay_rate.T
    residue_t = residue.T
    offsets = jnp.arange(tok_block, dtype=jnp.float32)
    to_end = outer_table(state_high, state_low)
    block_state = jnp.sum(to_end * driven[None, :, :], axis=2)
    rounds = blocks.bit_length() - 1
    assert 1 << rounds == blocks
    on_chip = chan_count.bit_length() - 1
    chunk_levels = [level for level in range(rounds) if level != on_chip][:4]
    pieces = len(chunk_levels)
    piece = channels // pieces
    span_rate = rate_t * tok_block
    carry_in = jnp.zeros_like(block_state)
    group_total = block_state
    direct = []
    for level in range(rounds):
        width = 1 << level
        if level in chunk_levels:
            lo = chunk_levels.index(level) * piece
            group_total, chunk_in = lax.optimization_barrier((group_total, driven[lo:lo + piece]))
        if level == on_chip:
            group_total, factor_rate = lax.optimization_barrier((group_total, rate_t))
        pairs = [(src_i, src_i ^ width) for src_i in range(blocks)]
        other = lax.ppermute(group_total, ("seq", "chan"), pairs)
        if level in chunk_levels:
            chunk_out = local_chunk(
                chunk_in, rate_t[:, lo:lo + piece], residue_t[:, lo:lo + piece], skip_gain[lo:lo + piece]
            )
        upper = (owner_idx & width) != 0
        place = (owner_idx % width).astype(jnp.float32)
        carry_in = jnp.where(upper, carry_in + jnp.exp(-span_rate * place) * other, carry_in)
        shrink = jnp.exp(-span_rate * width)
        if level == rounds - 1:
            own_w = residue_t * jnp.where(upper, 1.0, shrink)
            other_w = residue_t * jnp.where(upper, shrink, 1.0)
            own_part, other_w = lax.optimization_barrier((own_w * group_total, other_w))
            modal_t = own_part + other_w * other
        later = jnp.where(upper, group_total, other)
        earlier = jnp.where(upper, other, group_total)
        group_total = later + shrink * earlier
        if level == on_chip:
            carry_high, carry_low = lane_factors(factor_rate, 0.0, 1.0, tok_block)
            group_total, carry_in, carry_high, carry_low = lax.optimization_barrier(
                (group_total, carry_in, carry_high, carry_low)
            )
        if level in chunk_levels:
            group_total, carry_in, chunk_out = lax.optimization_barrier((group_total, carry_in, chunk_out))
            direct.append(chunk_out)
    modal_state = modal_t.T
    carry_coef = residue_t * jnp.exp(-rate_t) * carry_in
    weighted = carry_coef[:, None, :] * carry_high
    carry_t = jnp.sum(weighted[:, :, None, :] * carry_low[:, None, :, :], axis=0)
    carry_part = carry_t.reshape(tok_block, channels).T
    convolved = jnp.concatenate(direct, axis=0) + carry_part
    layer_out = (outer_gate.astype(jnp.float32) * convolved).astype(jnp.bfloat16)
    return (layer_out, modal_state)


def solution(mesh):
    placed = (
        P(None, ("seq", "chan")),
        P(None, ("seq", "chan")),
        P(None, ("seq", "chan")),
        P(),
        P(),
        P(),
    )
    return jax.shard_map(
        on_device,
        mesh=mesh,
        in_specs=placed,
        out_specs=(P(None, ("seq", "chan")), P()),
        check_vma=False,
    )
```

```python
import jax
import jax.numpy as jnp
from jax import lax
from jax.sharding import PartitionSpec as P


def prefix_matrix(length):
    rows = lax.iota(jnp.int32, length)
    return (rows[:, None] <= rows[None, :]).astype(jnp.bfloat16)


def prefix_sum(values, tri):
    upper = values.astype(jnp.bfloat16)
    lower = (values - upper.astype(jnp.float32)).astype(jnp.bfloat16)
    first = jnp.einsum("mcs,st->mct", upper, tri, preferred_element_type=jnp.float32)
    second = jnp.einsum("mcs,st->mct", lower, tri, preferred_element_type=jnp.float32)
    return first + second


def power_factors(rate_t, first, step):
    coarse = jnp.arange(16, dtype=jnp.float32) * (16.0 * step)
    fine = first + jnp.arange(16, dtype=jnp.float32) * step
    high = jnp.exp(-rate_t[:, :, None] * coarse[None, None, :])
    low = jnp.exp(-rate_t[:, :, None] * fine[None, None, :])
    return high, low


def outer_table(high, low):
    modes, channels = high.shape[:2]
    return (high[:, :, :, None] * low[:, :, None, :]).reshape(modes, channels, 256)


def power_table(rate_t, first, step):
    return outer_table(*power_factors(rate_t, first, step))


def local_chunk(driven, rate_t, residue_t, skip_gain):
    tok_block = driven.shape[1]
    offsets = jnp.arange(tok_block, dtype=jnp.float32)
    rising = jnp.exp(rate_t[:, :, None] * offsets[None, None, :])
    falling = jnp.exp(-rate_t[:, :, None] * offsets[None, None, :])
    running = prefix_sum(rising * driven[None, :, :], prefix_matrix(tok_block))
    local_part = jnp.sum(residue_t[:, :, None] * falling * running, axis=0)
    return local_part + skip_gain[:, None] * driven


def on_device(signal, inner_gate, outer_gate, decay_rate, residue, skip_gain):
    channels, tok_block = signal.shape
    seq_count = lax.axis_size("seq")
    chan_count = lax.axis_size("chan")
    blocks = seq_count * chan_count
    owner_idx = lax.axis_index("seq") * chan_count + lax.axis_index("chan")
    state_high, state_low = power_factors(decay_rate.T, tok_block - 1.0, -1.0)
    state_high, state_low, signal, inner_gate = lax.optimization_barrier(
        (state_high, state_low, signal, inner_gate)
    )
    gated_in = (inner_gate.astype(jnp.float32) * signal.astype(jnp.float32)).astype(jnp.bfloat16)
    driven = lax.optimization_barrier(gated_in).astype(jnp.float32)
    rate_t = decay_rate.T
    residue_t = residue.T
    offsets = jnp.arange(tok_block, dtype=jnp.float32)
    to_end = outer_table(state_high, state_low)
    block_state = jnp.sum(to_end * driven[None, :, :], axis=2)
    rounds = blocks.bit_length() - 1
    assert 1 << rounds == blocks
    on_chip = chan_count.bit_length() - 1
    chunk_levels = [level for level in range(rounds) if level != on_chip][:4]
    pieces = len(chunk_levels)
    piece = channels // pieces
    span_rate = rate_t * tok_block
    carry_in = jnp.zeros_like(block_state)
    group_total = block_state
    direct = []
    for level in range(rounds):
        width = 1 << level
        if level in chunk_levels:
            lo = chunk_levels.index(level) * piece
            group_total, chunk_in = lax.optimization_barrier((group_total, driven[lo:lo + piece]))
        pairs = [(src_i, src_i ^ width) for src_i in range(blocks)]
        other = lax.ppermute(group_total, ("seq", "chan"), pairs)
        if level in chunk_levels:
            chunk_out = local_chunk(
                chunk_in, rate_t[:, lo:lo + piece], residue_t[:, lo:lo + piece], skip_gain[lo:lo + piece]
            )
        upper = (owner_idx & width) != 0
        place = (owner_idx % width).astype(jnp.float32)
        carry_in = jnp.where(upper, carry_in + jnp.exp(-span_rate * place) * other, carry_in)
        shrink = jnp.exp(-span_rate * width)
        if level == rounds - 1:
            own_w = residue_t * jnp.where(upper, 1.0, shrink)
            other_w = residue_t * jnp.where(upper, shrink, 1.0)
            own_part, other_w = lax.optimization_barrier((own_w * group_total, other_w))
            modal_t = own_part + other_w * other
        later = jnp.where(upper, group_total, other)
        earlier = jnp.where(upper, other, group_total)
        group_total = later + shrink * earlier
        if level in chunk_levels:
            group_total, carry_in, chunk_out = lax.optimization_barrier((group_total, carry_in, chunk_out))
            direct.append(chunk_out)
    modal_t, carry_in = lax.optimization_barrier((modal_t, carry_in))
    modal_state = modal_t.T
    falling = power_table(rate_t, 0.0, 1.0)
    carry_coef = residue_t * jnp.exp(-rate_t) * carry_in
    carry_part = jnp.sum(carry_coef[:, :, None] * falling, axis=0)
    convolved = jnp.concatenate(direct, axis=0) + carry_part
    layer_out = (outer_gate.astype(jnp.float32) * convolved).astype(jnp.bfloat16)
    return (layer_out, modal_state)


def solution(mesh):
    placed = (
        P(None, ("seq", "chan")),
        P(None, ("seq", "chan")),
        P(None, ("seq", "chan")),
        P(),
        P(),
        P(),
    )
    return jax.shard_map(
        on_device,
        mesh=mesh,
        in_specs=placed,
        out_specs=(P(None, ("seq", "chan")), P()),
        check_vma=False,
    )
```

```python
import jax
import jax.numpy as jnp
from jax import lax
from jax.sharding import PartitionSpec as P


def prefix_matrix(length):
    rows = lax.iota(jnp.int32, length)
    return (rows[:, None] <= rows[None, :]).astype(jnp.bfloat16)


def prefix_sum(values, tri):
    upper = values.astype(jnp.bfloat16)
    lower = (values - upper.astype(jnp.float32)).astype(jnp.bfloat16)
    first = jnp.einsum("mcs,st->mct", upper, tri, preferred_element_type=jnp.float32)
    second = jnp.einsum("mcs,st->mct", lower, tri, preferred_element_type=jnp.float32)
    return first + second


def power_factors(rate_t, first, step):
    coarse = jnp.arange(16, dtype=jnp.float32) * (16.0 * step)
    fine = first + jnp.arange(16, dtype=jnp.float32) * step
    high = jnp.exp(-rate_t[:, :, None] * coarse[None, None, :])
    low = jnp.exp(-rate_t[:, :, None] * fine[None, None, :])
    return high, low


def outer_table(high, low):
    modes, channels = high.shape[:2]
    return (high[:, :, :, None] * low[:, :, None, :]).reshape(modes, channels, 256)


def power_table(rate_t, first, step):
    return outer_table(*power_factors(rate_t, first, step))


def local_chunk(driven, rate_t, residue_t, skip_gain):
    tok_block = driven.shape[1]
    offsets = jnp.arange(tok_block, dtype=jnp.float32)
    rising = jnp.exp(rate_t[:, :, None] * offsets[None, None, :])
    falling = jnp.exp(-rate_t[:, :, None] * offsets[None, None, :])
    running = prefix_sum(rising * driven[None, :, :], prefix_matrix(tok_block))
    local_part = jnp.sum(residue_t[:, :, None] * falling * running, axis=0)
    return local_part + skip_gain[:, None] * driven


def on_device(signal, inner_gate, outer_gate, decay_rate, residue, skip_gain):
    channels, tok_block = signal.shape
    seq_count = lax.axis_size("seq")
    chan_count = lax.axis_size("chan")
    blocks = seq_count * chan_count
    owner_idx = lax.axis_index("seq") * chan_count + lax.axis_index("chan")
    state_high, state_low = power_factors(decay_rate.T, tok_block - 1.0, -1.0)
    state_high, state_low, signal, inner_gate = lax.optimization_barrier(
        (state_high, state_low, signal, inner_gate)
    )
    gated_in = (inner_gate.astype(jnp.float32) * signal.astype(jnp.float32)).astype(jnp.bfloat16)
    driven = lax.optimization_barrier(gated_in).astype(jnp.float32)
    rate_t = decay_rate.T
    residue_t = residue.T
    offsets = jnp.arange(tok_block, dtype=jnp.float32)
    split = driven.reshape(channels, state_high.shape[2], state_low.shape[2])
    partial = jnp.sum(state_low[:, :, None, :] * split[None, :, :, :], axis=3)
    block_state = jnp.sum(state_high * partial, axis=2)
    rounds = blocks.bit_length() - 1
    assert 1 << rounds == blocks
    on_chip = chan_count.bit_length() - 1
    chunk_levels = [level for level in range(rounds) if level != on_chip][:4]
    pieces = len(chunk_levels)
    piece = channels // pieces
    span_rate = rate_t * tok_block
    carry_in = jnp.zeros_like(block_state)
    group_total = block_state
    direct = []
    for level in range(rounds):
        width = 1 << level
        if level in chunk_levels:
            lo = chunk_levels.index(level) * piece
            group_total, chunk_in = lax.optimization_barrier((group_total, driven[lo:lo + piece]))
        pairs = [(src_i, src_i ^ width) for src_i in range(blocks)]
        other = lax.ppermute(group_total, ("seq", "chan"), pairs)
        if level in chunk_levels:
            chunk_out = local_chunk(
                chunk_in, rate_t[:, lo:lo + piece], residue_t[:, lo:lo + piece], skip_gain[lo:lo + piece]
            )
        upper = (owner_idx & width) != 0
        place = (owner_idx % width).astype(jnp.float32)
        carry_in = jnp.where(upper, carry_in + jnp.exp(-span_rate * place) * other, carry_in)
        shrink = jnp.exp(-span_rate * width)
        if level == rounds - 1:
            own_w = residue_t * jnp.where(upper, 1.0, shrink)
            other_w = residue_t * jnp.where(upper, shrink, 1.0)
            own_part, other_w = lax.optimization_barrier((own_w * group_total, other_w))
            modal_t = own_part + other_w * other
        later = jnp.where(upper, group_total, other)
        earlier = jnp.where(upper, other, group_total)
        group_total = later + shrink * earlier
        if level in chunk_levels:
            group_total, carry_in, chunk_out = lax.optimization_barrier((group_total, carry_in, chunk_out))
            direct.append(chunk_out)
    modal_state = modal_t.T
    falling = power_table(rate_t, 0.0, 1.0)
    carry_coef = residue_t * jnp.exp(-rate_t) * carry_in
    carry_part = jnp.sum(carry_coef[:, :, None] * falling, axis=0)
    convolved = jnp.concatenate(direct, axis=0) + carry_part
    layer_out = (outer_gate.astype(jnp.float32) * convolved).astype(jnp.bfloat16)
    return (layer_out, modal_state)


def solution(mesh):
    placed = (
        P(None, ("seq", "chan")),
        P(None, ("seq", "chan")),
        P(None, ("seq", "chan")),
        P(),
        P(),
        P(),
    )
    return jax.shard_map(
        on_device,
        mesh=mesh,
        in_specs=placed,
        out_specs=(P(None, ("seq", "chan")), P()),
        check_vma=False,
    )
```
